1024 devices in a mesh: domain: 32 (over z, x_lo), band: 32 (over y, x_hi, core).
Axes of the slice: x: 4 (x_hi: 2, x_lo: 2; x = x_hi * 2 + x_lo), y: 8, z: 16, core: 2. Of those that a mesh axis runs over, the one named last changes fastest.
Arguments:
- orbitals: float32 [96, 192, 16, 128], P('band', 'domain'), may hold values from -8.8 to 8.8
- potential: float32 [192, 16, 128], P('domain', None, 'band'), may hold values from -1.5 to 0
Outputs:
- filtered: float32 [96, 192, 16, 128], P('band', 'domain')
- intersection: float32 [96, 96], P('band')
- hamiltonian: float32 [96, 96], P('band')
The draws below stay inside these ranges and needn't reach their ends.
All inputs are finite; a program needn't handle non-finite values.
Results may differ from the reference program's by a relative error of at most 0.00005.
Values sent between devices are 32-bit elements; how exact they have to be, the bound alone decides.
No kernel may reach another device: no remote copies, remote signals or barrier semaphores. Data moves between devices by JAX's collectives and lax.ppermute only.
A program may use at most 32 MiB of HBM per device.

```python
import jax
import jax.numpy as jnp
from jax import lax

ORB = 96
DEGREE = 8
NY = 16
NZ = 128
NX = 192
CELLS = 393216


def draw_orbitals(key, part):
    base = jax.random.fold_in(key, 11)
    key_weight, key_common, key_private = jax.random.split(base, 3)
    weights = jax.random.uniform(key_weight, (ORB, 1, 1, 1), jnp.float32, 0.4, 1.2)
    private = jnp.clip(jax.random.normal(key_private, (ORB, NX, NY, NZ), jnp.float32), -4.0, 4.0)
    common = jnp.clip(jax.random.normal(key_common, (1, NX, NY, NZ), jnp.float32), -4.0, 4.0)
    return private + weights * common


def steps_of(own_key, dims, shards, least, largest):
    gain = 1.0
    for axis_at, parts in shards:
        draws = jax.random.uniform(jax.random.fold_in(jax.random.fold_in(own_key, 6), axis_at), (parts,), jnp.float32, least / len(shards), largest / len(shards))
        gain = gain * jnp.repeat(jnp.exp(draws), dims[axis_at] // parts).reshape((-1,) + (1,) * (len(dims) - 1 - axis_at))
    return gain


def setup_inputs(seed: int = 0) -> dict:
    arg_keys = jax.random.split(jax.random.key(seed), 3)
    return {
        "orbitals": draw_orbitals(jax.random.fold_in(arg_keys[2], 71), 0),
        "potential": jnp.clip(-1.5 + 1.5 * jax.random.uniform(arg_keys[1], (NX, NY, NZ), jnp.float32) ** steps_of(arg_keys[1], (NX, NY, NZ), ((0, 32), (2, 32)), -0.2, 0.2), -1.5, 0.0),
    }


stencil_coeffs = (-5369.0 / 1800.0, 12.0 / 7.0, -15.0 / 56.0, 10.0 / 189.0, -1.0 / 112.0, 2.0 / 1925.0, -1.0 / 16632.0)
stencil_reach = 6
lower_bound = 4.5
upper_bound = 15.5
lowest_bound = 1.0


def laplace(grid_field):
    reach = stencil_reach
    size_y = grid_field.shape[2]
    size_z = grid_field.shape[3]
    padded_yz = jnp.pad(grid_field, ((0, 0), (0, 0), (reach, reach), (reach, reach)))
    summed = (3.0 * stencil_coeffs[0]) * grid_field
    for offset in range(1, reach + 1):
        along_x = jnp.roll(grid_field, -offset, 1) + jnp.roll(grid_field, offset, 1)
        along_y = padded_yz[:, :, reach + offset:reach + offset + size_y, reach:reach + size_z] + padded_yz[:, :, reach - offset:reach - offset + size_y, reach:reach + size_z]
        along_z = padded_yz[:, :, reach:reach + size_y, reach + offset:reach + offset + size_z] + padded_yz[:, :, reach:reach + size_y, reach - offset:reach - offset + size_z]
        summed = summed + stencil_coeffs[offset] * (along_x + along_y + along_z)
    return summed


def apply_hamiltonian(grid_field, potential):
    return -0.5 * laplace(grid_field) + potential[None] * grid_field


def contract(left, right):
    return lax.dot_general(left, right, (((1,), (1,)), ((), ())), precision=lax.Precision.HIGHEST, preferred_element_type=jnp.float32)


def reference(orbitals, potential):
    half_width = (upper_bound - lower_bound) / 2.0
    centre = (upper_bound + lower_bound) / 2.0
    sigma_first = half_width / (lowest_bound - centre)
    previous = orbitals
    current = (apply_hamiltonian(previous, potential) - centre * previous) * (sigma_first / half_width)
    sigma_now = sigma_first
    for degree_step in range(2, DEGREE + 1):
        sigma_next = 1.0 / (2.0 / sigma_first - sigma_now)
        update = (apply_hamiltonian(current, potential) - centre * current) * (2.0 * sigma_next / half_width) - (sigma_now * sigma_next) * previous
        previous = current
        current = update
        sigma_now = sigma_next
    filtered = current
    h_image = apply_hamiltonian(filtered, potential)
    flat_panel = filtered.reshape(ORB, -1)
    flat_image = h_image.reshape(ORB, -1)
    intersection = contract(flat_panel, flat_panel) / CELLS
    hamiltonian = contract(flat_image, flat_panel) / CELLS
    return filtered, intersection, hamiltonian
```

```python
import jax
import jax.numpy as jnp
from jax import lax
from jax.sharding import PartitionSpec as P

DEGREE = 8


stencil_coeffs = (
    -5369.0 / 1800.0,
    12.0 / 7.0,
    -15.0 / 56.0,
    10.0 / 189.0,
    -1.0 / 112.0,
    2.0 / 1925.0,
    -1.0 / 16632.0,
)
stencil_reach = 6
lower_bound = 4.5
upper_bound = 15.5
lowest_bound = 1.0


def extended(cells, sides, width):
    for axis, dim in sides:
        count = lax.axis_size(axis)
        head = lax.slice_in_dim(cells, 0, width, axis=dim)
        tail = lax.slice_in_dim(cells, cells.shape[dim] - width, cells.shape[dim], axis=dim)
        cells = jnp.concatenate(
            [
                lax.ppermute(tail, axis, [(i, (i + 1) % count) for i in range(count)]),
                cells,
                lax.ppermute(head, axis, [((i + 1) % count, i) for i in range(count)]),
            ],
            axis=dim,
        )
    return cells


def laplace(grid_field):
    planes = grid_field.shape[1]
    size_y = grid_field.shape[2]
    size_z = grid_field.shape[3]
    padded_x = extended(grid_field, (("domain", 1),), 6)
    padded_yz = jnp.pad(
        grid_field, ((0, 0), (0, 0), (stencil_reach, stencil_reach), (stencil_reach, stencil_reach))
    )
    summed = 3.0 * stencil_coeffs[0] * grid_field
    for offset in range(1, stencil_reach + 1):
        along_x = (
            padded_x[:, stencil_reach + offset : stencil_reach + offset + planes]
            + padded_x[:, stencil_reach - offset : stencil_reach - offset + planes]
        )
        along_y = (
            padded_yz[
                :,
                :,
                stencil_reach + offset : stencil_reach + offset + size_y,
                stencil_reach : stencil_reach + size_z,
            ]
            + padded_yz[
                :,
                :,
                stencil_reach - offset : stencil_reach - offset + size_y,
                stencil_reach : stencil_reach + size_z,
            ]
        )
        along_z = (
            padded_yz[
                :,
                :,
                stencil_reach : stencil_reach + size_y,
                stencil_reach + offset : stencil_reach + offset + size_z,
            ]
            + padded_yz[
                :,
                :,
                stencil_reach : stencil_reach + size_y,
                stencil_reach - offset : stencil_reach - offset + size_z,
            ]
        )
        summed = summed + stencil_coeffs[offset] * (along_x + along_y + along_z)
    return summed


def apply_hamiltonian(grid_field, local_pot):
    return -0.5 * laplace(grid_field) + local_pot[None] * grid_field


def contract(left, right):
    return lax.dot_general(
        left,
        right,
        (((1,), (1,)), ((), ())),
        precision=lax.Precision.HIGHEST,
        preferred_element_type=jnp.float32,
    )


def gather_potential(potential):
    parts = lax.axis_size("band")
    sent = jnp.broadcast_to(potential[None], (parts,) + potential.shape)
    got = lax.all_to_all(sent, "band", 0, 0, tiled=True)
    planes, size_y, slab = potential.shape
    return got.transpose(1, 2, 0, 3).reshape(planes, size_y, parts * slab)


def gram_rows(flat_panel, flat_image):
    parts = lax.axis_size("band")
    orb_dev, cells = flat_panel.shape
    share = cells // parts
    both = jnp.concatenate([flat_panel, flat_image], axis=0)
    both = both.reshape(2 * orb_dev, parts, share).transpose(1, 0, 2)
    got = lax.all_to_all(both, "band", 0, 0, tiled=True)
    panel_all = got[:, :orb_dev].reshape(parts * orb_dev, share)
    image_all = got[:, orb_dev:].reshape(parts * orb_dev, share)
    s_part = contract(panel_all, panel_all)
    h_part = contract(image_all, panel_all)
    tiles = jnp.stack([s_part, h_part]).reshape(2, parts, orb_dev, parts * orb_dev)
    got = lax.all_to_all(tiles.transpose(1, 0, 2, 3), "band", 0, 0, tiled=True)
    rows = jnp.sum(got, axis=0)
    count = lax.axis_size("domain")
    sent = jnp.broadcast_to(rows[None], (count,) + rows.shape)
    got = lax.all_to_all(sent, "domain", 0, 0, tiled=True)
    return jnp.sum(got, axis=0)


def body(orbitals, potential):
    local_pot = gather_potential(potential)
    half_width = (upper_bound - lower_bound) / 2.0
    centre = (upper_bound + lower_bound) / 2.0
    sigma_first = half_width / (lowest_bound - centre)
    previous = orbitals
    current = (apply_hamiltonian(previous, local_pot) - centre * previous) * (
        sigma_first / half_width
    )
    sigma_now = sigma_first
    for degree_step in range(2, DEGREE + 1):
        sigma_next = 1.0 / (2.0 / sigma_first - sigma_now)
        update = (apply_hamiltonian(current, local_pot) - centre * current) * (
            2.0 * sigma_next / half_width
        ) - sigma_now * sigma_next * previous
        previous = current
        current = update
        sigma_now = sigma_next
    h_image = apply_hamiltonian(current, local_pot)
    orb_dev = current.shape[0]
    cell_count = current.shape[1] * current.shape[2] * current.shape[3] * lax.axis_size("domain")
    totals = gram_rows(current.reshape(orb_dev, -1), h_image.reshape(orb_dev, -1))
    intersection = totals[0] / cell_count
    hamiltonian = totals[1] / cell_count
    return (current, intersection, hamiltonian)


def solution(mesh):
    placed = (P("band", "domain", None, None), P("domain", None, "band"))
    return jax.shard_map(
        body,
        mesh=mesh,
        in_specs=placed,
        out_specs=(P("band", "domain", None, None), P("band", None), P("band", None)),
        check_vma=False,
    )
```

```python
import jax
import jax.numpy as jnp
from jax import lax
from jax.sharding import PartitionSpec as P

DEGREE = 8


stencil_coeffs = (
    -5369.0 / 1800.0,
    12.0 / 7.0,
    -15.0 / 56.0,
    10.0 / 189.0,
    -1.0 / 112.0,
    2.0 / 1925.0,
    -1.0 / 16632.0,
)
stencil_reach = 6
lower_bound = 4.5
upper_bound = 15.5
lowest_bound = 1.0


def extended(cells, sides, width):
    for axis, dim in sides:
        count = lax.axis_size(axis)
        head = lax.slice_in_dim(cells, 0, width, axis=dim)
        tail = lax.slice_in_dim(cells, cells.shape[dim] - width, cells.shape[dim], axis=dim)
        cells = jnp.concatenate(
            [
                lax.ppermute(tail, axis, [(i, (i + 1) % count) for i in range(count)]),
                cells,
                lax.ppermute(head, axis, [((i + 1) % count, i) for i in range(count)]),
            ],
            axis=dim,
        )
    return cells


def laplace(grid_field):
    planes = grid_field.shape[1]
    size_y = grid_field.shape[2]
    size_z = grid_field.shape[3]
    padded_x = extended(grid_field, (("domain", 1),), 6)
    padded_yz = jnp.pad(
        grid_field, ((0, 0), (0, 0), (stencil_reach, stencil_reach), (stencil_reach, stencil_reach))
    )
    summed = 3.0 * stencil_coeffs[0] * grid_field
    for offset in range(1, stencil_reach + 1):
        along_x = (
            padded_x[:, stencil_reach + offset : stencil_reach + offset + planes]
            + padded_x[:, stencil_reach - offset : stencil_reach - offset + planes]
        )
        along_y = (
            padded_yz[
                :,
                :,
                stencil_reach + offset : stencil_reach + offset + size_y,
                stencil_reach : stencil_reach + size_z,
            ]
            + padded_yz[
                :,
                :,
                stencil_reach - offset : stencil_reach - offset + size_y,
                stencil_reach : stencil_reach + size_z,
            ]
        )
        along_z = (
            padded_yz[
                :,
                :,
                stencil_reach : stencil_reach + size_y,
                stencil_reach + offset : stencil_reach + offset + size_z,
            ]
            + padded_yz[
                :,
                :,
                stencil_reach : stencil_reach + size_y,
                stencil_reach - offset : stencil_reach - offset + size_z,
            ]
        )
        summed = summed + stencil_coeffs[offset] * (along_x + along_y + along_z)
    return summed


def apply_hamiltonian(grid_field, local_pot):
    return -0.5 * laplace(grid_field) + local_pot[None] * grid_field


def contract(left, right):
    return lax.dot_general(
        left,
        right,
        (((1,), (1,)), ((), ())),
        precision=lax.Precision.HIGHEST,
        preferred_element_type=jnp.float32,
    )


def gather_potential(potential):
    parts = lax.axis_size("band")
    sent = jnp.broadcast_to(potential[None], (parts,) + potential.shape)
    got = lax.all_to_all(sent, "band", 0, 0, tiled=True)
    planes, size_y, slab = potential.shape
    return got.transpose(1, 2, 0, 3).reshape(planes, size_y, parts * slab)


def gram_rows(flat_panel, flat_image):
    parts = lax.axis_size("band")
    orb_dev, cells = flat_panel.shape
    share = cells // parts
    both = jnp.concatenate([flat_panel, flat_image], axis=0)
    both = both.reshape(2 * orb_dev, parts, share).transpose(1, 0, 2)
    got = lax.all_to_all(both, "band", 0, 0, tiled=True)
    panel_all = got[:, :orb_dev].reshape(parts * orb_dev, share)
    image_all = got[:, orb_dev:].reshape(parts * orb_dev, share)
    s_part = contract(panel_all, panel_all)
    h_part = contract(image_all, panel_all)
    tiles = jnp.stack([s_part, h_part]).reshape(2, parts, orb_dev, parts * orb_dev)
    got = lax.all_to_all(tiles.transpose(1, 0, 2, 3), "band", 0, 0, tiled=True)
    rows = jnp.sum(got, axis=0)
    count = lax.axis_size("domain")
    sent = jnp.broadcast_to(rows[None], (count,) + rows.shape)
    got = lax.all_to_all(sent, "domain", 0, 0, tiled=True)
    return jnp.sum(got, axis=0)


def halo_of(fields, depths, planes):
    count = lax.axis_size("domain")
    reach = max(depths)
    blocks = -(-reach // planes)
    lefts = [[] for _ in fields]
    rights = [[] for _ in fields]
    for shift in range(1, blocks + 1):
        wanted = [i for i, depth in enumerate(depths) if depth > (shift - 1) * planes]
        packed = jnp.concatenate([fields[i] for i in wanted], axis=0)
        from_left = lax.ppermute(packed, "domain", [(i, (i + shift) % count) for i in range(count)])
        from_right = lax.ppermute(packed, "domain", [(i, (i - shift) % count) for i in range(count)])
        row = 0
        for i in wanted:
            rows = fields[i].shape[0]
            lefts[i].insert(0, from_left[row : row + rows])
            rights[i].append(from_right[row : row + rows])
            row += rows
    out = []
    for i, depth in enumerate(depths):
        wide = jnp.concatenate(lefts[i] + [fields[i]] + rights[i], axis=1)
        cut = len(lefts[i]) * planes - depth
        out.append(lax.slice_in_dim(wide, cut, wide.shape[1] - cut, axis=1))
    return out


def crop(field, depth):
    return lax.slice_in_dim(field, depth, field.shape[1] - depth, axis=1)


def laplace_inner(grid_field):
    planes = grid_field.shape[1] - 2 * stencil_reach
    size_y = grid_field.shape[2]
    size_z = grid_field.shape[3]
    inner = crop(grid_field, stencil_reach)
    padded_yz = jnp.pad(
        inner, ((0, 0), (0, 0), (stencil_reach, stencil_reach), (stencil_reach, stencil_reach))
    )
    summed = 3.0 * stencil_coeffs[0] * inner
    for offset in range(1, stencil_reach + 1):
        along_x = (
            grid_field[:, stencil_reach + offset : stencil_reach + offset + planes]
            + grid_field[:, stencil_reach - offset : stencil_reach - offset + planes]
        )
        along_y = (
            padded_yz[
                :,
                :,
                stencil_reach + offset : stencil_reach + offset + size_y,
                stencil_reach : stencil_reach + size_z,
            ]
            + padded_yz[
                :,
                :,
                stencil_reach - offset : stencil_reach - offset + size_y,
                stencil_reach : stencil_reach + size_z,
            ]
        )
        along_z = (
            padded_yz[
                :,
                :,
                stencil_reach : stencil_reach + size_y,
                stencil_reach + offset : stencil_reach + offset + size_z,
            ]
            + padded_yz[
                :,
                :,
                stencil_reach : stencil_reach + size_y,
                stencil_reach - offset : stencil_reach - offset + size_z,
            ]
        )
        summed = summed + stencil_coeffs[offset] * (along_x + along_y + along_z)
    return summed


def hamiltonian_inner(grid_field, wide_pot):
    inner = crop(grid_field, stencil_reach)
    cut = (wide_pot.shape[0] - inner.shape[1]) // 2
    pot = lax.slice_in_dim(wide_pot, cut, wide_pot.shape[0] - cut, axis=0)
    return -0.5 * laplace_inner(grid_field) + pot[None] * inner


def body(orbitals, potential):
    local_pot = gather_potential(potential)
    planes = orbitals.shape[1]
    half_width = (upper_bound - lower_bound) / 2.0
    centre = (upper_bound + lower_bound) / 2.0
    sigma_first = half_width / (lowest_bound - centre)
    per_phase = 3
    applications = DEGREE + 1
    pot_depth = stencil_reach * (per_phase - 1)
    current, wide_pot = halo_of([orbitals, local_pot[None]], [stencil_reach * per_phase, pot_depth], planes)
    wide_pot = wide_pot[0]
    previous = None
    sigma_now = sigma_first
    step = 0
    h_image = None
    while step < applications:
        if step > 0:
            todo = min(per_phase, applications - step)
            if previous is not None and step < DEGREE:
                current, previous = halo_of(
                    [current, previous], [stencil_reach * todo, stencil_reach * (todo - 1)], planes
                )
            else:
                (current,) = halo_of([current], [stencil_reach * todo], planes)
        else:
            todo = per_phase
        for _ in range(todo):
            if step == 0:
                previous = current
                current = (hamiltonian_inner(current, wide_pot) - centre * crop(current, stencil_reach)) * (
                    sigma_first / half_width
                )
            elif step < DEGREE:
                sigma_next = 1.0 / (2.0 / sigma_first - sigma_now)
                inner = crop(current, stencil_reach)
                lag = (previous.shape[1] - inner.shape[1]) // 2
                update = (hamiltonian_inner(current, wide_pot) - centre * inner) * (
                    2.0 * sigma_next / half_width
                ) - sigma_now * sigma_next * crop(previous, lag)
                previous = current
                current = update
                sigma_now = sigma_next
            else:
                h_image = hamiltonian_inner(current, wide_pot)
            step += 1
        if step < applications:
            lag = (previous.shape[1] - planes) // 2
            previous = crop(previous, lag)
    depth = (current.shape[1] - planes) // 2
    current = crop(current, depth)
    orb_dev = current.shape[0]
    cell_count = current.shape[1] * current.shape[2] * current.shape[3] * lax.axis_size("domain")
    totals = gram_rows(current.reshape(orb_dev, -1), h_image.reshape(orb_dev, -1))
    intersection = totals[0] / cell_count
    hamiltonian = totals[1] / cell_count
    return (current, intersection, hamiltonian)


def solution(mesh):
    placed = (P("band", "domain", None, None), P("domain", None, "band"))
    return jax.shard_map(
        body,
        mesh=mesh,
        in_specs=placed,
        out_specs=(P("band", "domain", None, None), P("band", None), P("band", None)),
        check_vma=False,
    )
```

```python
import jax
import jax.numpy as jnp
from jax import lax
from jax.sharding import PartitionSpec as P

DEGREE = 8


stencil_coeffs = (
    -5369.0 / 1800.0,
    12.0 / 7.0,
    -15.0 / 56.0,
    10.0 / 189.0,
    -1.0 / 112.0,
    2.0 / 1925.0,
    -1.0 / 16632.0,
)
stencil_reach = 6
lower_bound = 4.5
upper_bound = 15.5
lowest_bound = 1.0


def extended(cells, sides, width):
    for axis, dim in sides:
        count = lax.axis_size(axis)
        head = lax.slice_in_dim(cells, 0, width, axis=dim)
        tail = lax.slice_in_dim(cells, cells.shape[dim] - width, cells.shape[dim], axis=dim)
        cells = jnp.concatenate(
            [
                lax.ppermute(tail, axis, [(i, (i + 1) % count) for i in range(count)]),
                cells,
                lax.ppermute(head, axis, [((i + 1) % count, i) for i in range(count)]),
            ],
            axis=dim,
        )
    return cells


def laplace(grid_field):
    planes = grid_field.shape[1]
    size_y = grid_field.shape[2]
    size_z = grid_field.shape[3]
    padded_x = extended(grid_field, (("domain", 1),), 6)
    padded_yz = jnp.pad(
        grid_field, ((0, 0), (0, 0), (stencil_reach, stencil_reach), (stencil_reach, stencil_reach))
    )
    summed = 3.0 * stencil_coeffs[0] * grid_field
    for offset in range(1, stencil_reach + 1):
        along_x = (
            padded_x[:, stencil_reach + offset : stencil_reach + offset + planes]
            + padded_x[:, stencil_reach - offset : stencil_reach - offset + planes]
        )
        along_y = (
            padded_yz[
                :,
                :,
                stencil_reach + offset : stencil_reach + offset + size_y,
                stencil_reach : stencil_reach + size_z,
            ]
            + padded_yz[
                :,
                :,
                stencil_reach - offset : stencil_reach - offset + size_y,
                stencil_reach : stencil_reach + size_z,
            ]
        )
        along_z = (
            padded_yz[
                :,
                :,
                stencil_reach : stencil_reach + size_y,
                stencil_reach + offset : stencil_reach + offset + size_z,
            ]
            + padded_yz[
                :,
                :,
                stencil_reach : stencil_reach + size_y,
                stencil_reach - offset : stencil_reach - offset + size_z,
            ]
        )
        summed = summed + stencil_coeffs[offset] * (along_x + along_y + along_z)
    return summed


def apply_hamiltonian(grid_field, local_pot):
    return -0.5 * laplace(grid_field) + local_pot[None] * grid_field


def contract(left, right):
    return lax.dot_general(
        left,
        right,
        (((1,), (1,)), ((), ())),
        precision=lax.Precision.HIGHEST,
        preferred_element_type=jnp.float32,
    )


def gather_potential(potential):
    parts = lax.axis_size("band")
    sent = jnp.broadcast_to(potential[None], (parts,) + potential.shape)
    got = lax.all_to_all(sent, "band", 0, 0, tiled=True)
    planes, size_y, slab = potential.shape
    return got.transpose(1, 2, 0, 3).reshape(planes, size_y, parts * slab)


def gram_rows(flat_panel, flat_image):
    parts = lax.axis_size("band")
    orb_dev, cells = flat_panel.shape
    share = cells // parts
    both = jnp.concatenate([flat_panel, flat_image], axis=0)
    both = both.reshape(2 * orb_dev, parts, share).transpose(1, 0, 2)
    got = lax.all_to_all(both, "band", 0, 0, tiled=True)
    panel_all = got[:, :orb_dev].reshape(parts * orb_dev, share)
    image_all = got[:, orb_dev:].reshape(parts * orb_dev, share)
    s_part = contract(panel_all, panel_all)
    h_part = contract(image_all, panel_all)
    tiles = jnp.stack([s_part, h_part]).reshape(2, parts, orb_dev, parts * orb_dev)
    got = lax.all_to_all(tiles.transpose(1, 0, 2, 3), "band", 0, 0, tiled=True)
    rows = jnp.sum(got, axis=0)
    count = lax.axis_size("domain")
    sent = jnp.broadcast_to(rows[None], (count,) + rows.shape)
    got = lax.all_to_all(sent, "domain", 0, 0, tiled=True)
    return jnp.sum(got, axis=0)


def halo_of(fields, depths, planes):
    count = lax.axis_size("domain")
    blocks = -(-max(depths) // planes)
    rows = [field.shape[0] for field in fields]
    stack = jnp.concatenate(fields, axis=0)
    have = 0
    while have < blocks:
        shift = 2 * have + 1
        from_left = lax.ppermute(stack, "domain", [(i, (i + shift) % count) for i in range(count)])
        from_right = lax.ppermute(stack, "domain", [(i, (i - shift) % count) for i in range(count)])
        stack = jnp.concatenate([from_left, stack, from_right], axis=1)
        have = 3 * have + 1
    out = []
    row = 0
    for count_rows, depth in zip(rows, depths):
        cut = have * planes - depth
        part = stack[row : row + count_rows]
        out.append(lax.slice_in_dim(part, cut, part.shape[1] - cut, axis=1))
        row += count_rows
    return out


def crop(field, depth):
    return lax.slice_in_dim(field, depth, field.shape[1] - depth, axis=1)


def laplace_inner(grid_field):
    planes = grid_field.shape[1] - 2 * stencil_reach
    size_y = grid_field.shape[2]
    size_z = grid_field.shape[3]
    inner = crop(grid_field, stencil_reach)
    padded_yz = jnp.pad(
        inner, ((0, 0), (0, 0), (stencil_reach, stencil_reach), (stencil_reach, stencil_reach))
    )
    summed = 3.0 * stencil_coeffs[0] * inner
    for offset in range(1, stencil_reach + 1):
        along_x = (
            grid_field[:, stencil_reach + offset : stencil_reach + offset + planes]
            + grid_field[:, stencil_reach - offset : stencil_reach - offset + planes]
        )
        along_y = (
            padded_yz[
                :,
                :,
                stencil_reach + offset : stencil_reach + offset + size_y,
                stencil_reach : stencil_reach + size_z,
            ]
            + padded_yz[
                :,
                :,
                stencil_reach - offset : stencil_reach - offset + size_y,
                stencil_reach : stencil_reach + size_z,
            ]
        )
        along_z = (
            padded_yz[
                :,
                :,
                stencil_reach : stencil_reach + size_y,
                stencil_reach + offset : stencil_reach + offset + size_z,
            ]
            + padded_yz[
                :,
                :,
                stencil_reach : stencil_reach + size_y,
                stencil_reach - offset : stencil_reach - offset + size_z,
            ]
        )
        summed = summed + stencil_coeffs[offset] * (along_x + along_y + along_z)
    return summed


def hamiltonian_inner(grid_field, wide_pot):
    inner = crop(grid_field, stencil_reach)
    cut = (wide_pot.shape[0] - inner.shape[1]) // 2
    pot = lax.slice_in_dim(wide_pot, cut, wide_pot.shape[0] - cut, axis=0)
    return -0.5 * laplace_inner(grid_field) + pot[None] * inner


def body(orbitals, potential):
    local_pot = gather_potential(potential)
    planes = orbitals.shape[1]
    half_width = (upper_bound - lower_bound) / 2.0
    centre = (upper_bound + lower_bound) / 2.0
    sigma_first = half_width / (lowest_bound - centre)
    per_phase = 4
    applications = DEGREE + 1
    pot_depth = stencil_reach * (per_phase - 1)
    current, wide_pot = halo_of([orbitals, local_pot[None]], [stencil_reach * per_phase, pot_depth], planes)
    wide_pot = wide_pot[0]
    previous = None
    sigma_now = sigma_first
    step = 0
    h_image = None
    while step < applications:
        if step > 0:
            todo = min(per_phase, applications - step)
            if previous is not None and step < DEGREE:
                current, previous = halo_of(
                    [current, previous], [stencil_reach * todo, stencil_reach * (todo - 1)], planes
                )
            else:
                (current,) = halo_of([current], [stencil_reach * todo], planes)
        else:
            todo = per_phase
        for _ in range(todo):
            if step == 0:
                previous = current
                current = (hamiltonian_inner(current, wide_pot) - centre * crop(current, stencil_reach)) * (
                    sigma_first / half_width
                )
            elif step < DEGREE:
                sigma_next = 1.0 / (2.0 / sigma_first - sigma_now)
                inner = crop(current, stencil_reach)
                lag = (previous.shape[1] - inner.shape[1]) // 2
                update = (hamiltonian_inner(current, wide_pot) - centre * inner) * (
                    2.0 * sigma_next / half_width
                ) - sigma_now * sigma_next * crop(previous, lag)
                previous = current
                current = update
                sigma_now = sigma_next
            else:
                h_image = hamiltonian_inner(current, wide_pot)
            step += 1
        if step < applications:
            lag = (previous.shape[1] - planes) // 2
            previous = crop(previous, lag)
    depth = (current.shape[1] - planes) // 2
    current = crop(current, depth)
    orb_dev = current.shape[0]
    cell_count = current.shape[1] * current.shape[2] * current.shape[3] * lax.axis_size("domain")
    totals = gram_rows(current.reshape(orb_dev, -1), h_image.reshape(orb_dev, -1))
    intersection = totals[0] / cell_count
    hamiltonian = totals[1] / cell_count
    return (current, intersection, hamiltonian)


def solution(mesh):
    placed = (P("band", "domain", None, None), P("domain", None, "band"))
    return jax.shard_map(
        body,
        mesh=mesh,
        in_specs=placed,
        out_specs=(P("band", "domain", None, None), P("band", None), P("band", None)),
        check_vma=False,
    )
```

```python
import jax
import jax.numpy as jnp
from jax import lax
from jax.sharding import PartitionSpec as P

DEGREE = 8


stencil_coeffs = (
    -5369.0 / 1800.0,
    12.0 / 7.0,
    -15.0 / 56.0,
    10.0 / 189.0,
    -1.0 / 112.0,
    2.0 / 1925.0,
    -1.0 / 16632.0,
)
stencil_reach = 6
lower_bound = 4.5
upper_bound = 15.5
lowest_bound = 1.0


def extended(cells, sides, width):
    for axis, dim in sides:
        count = lax.axis_size(axis)
        head = lax.slice_in_dim(cells, 0, width, axis=dim)
        tail = lax.slice_in_dim(cells, cells.shape[dim] - width, cells.shape[dim], axis=dim)
        cells = jnp.concatenate(
            [
                lax.ppermute(tail, axis, [(i, (i + 1) % count) for i in range(count)]),
                cells,
                lax.ppermute(head, axis, [((i + 1) % count, i) for i in range(count)]),
            ],
            axis=dim,
        )
    return cells


def laplace(grid_field):
    planes = grid_field.shape[1]
    size_y = grid_field.shape[2]
    size_z = grid_field.shape[3]
    padded_x = extended(grid_field, (("domain", 1),), 6)
    padded_yz = jnp.pad(
        grid_field, ((0, 0), (0, 0), (stencil_reach, stencil_reach), (stencil_reach, stencil_reach))
    )
    summed = 3.0 * stencil_coeffs[0] * grid_field
    for offset in range(1, stencil_reach + 1):
        along_x = (
            padded_x[:, stencil_reach + offset : stencil_reach + offset + planes]
            + padded_x[:, stencil_reach - offset : stencil_reach - offset + planes]
        )
        along_y = (
            padded_yz[
                :,
                :,
                stencil_reach + offset : stencil_reach + offset + size_y,
                stencil_reach : stencil_reach + size_z,
            ]
            + padded_yz[
                :,
                :,
                stencil_reach - offset : stencil_reach - offset + size_y,
                stencil_reach : stencil_reach + size_z,
            ]
        )
        along_z = (
            padded_yz[
                :,
                :,
                stencil_reach : stencil_reach + size_y,
                stencil_reach + offset : stencil_reach + offset + size_z,
            ]
            + padded_yz[
                :,
                :,
                stencil_reach : stencil_reach + size_y,
                stencil_reach - offset : stencil_reach - offset + size_z,
            ]
        )
        summed = summed + stencil_coeffs[offset] * (along_x + along_y + along_z)
    return summed


def apply_hamiltonian(grid_field, local_pot):
    return -0.5 * laplace(grid_field) + local_pot[None] * grid_field


def contract(left, right):
    return lax.dot_general(
        left,
        right,
        (((1,), (1,)), ((), ())),
        precision=lax.Precision.HIGHEST,
        preferred_element_type=jnp.float32,
    )


def gather_potential(potential):
    parts = lax.axis_size("band")
    sent = jnp.broadcast_to(potential[None], (parts,) + potential.shape)
    got = lax.all_to_all(sent, "band", 0, 0, tiled=True)
    planes, size_y, slab = potential.shape
    return got.transpose(1, 2, 0, 3).reshape(planes, size_y, parts * slab)


def gram_rows(flat_panel, flat_image):
    parts = lax.axis_size("band")
    orb_dev, cells = flat_panel.shape
    share = cells // parts
    both = jnp.concatenate([flat_panel, flat_image], axis=0)
    both = both.reshape(2 * orb_dev, parts, share).transpose(1, 0, 2)
    got = lax.all_to_all(both, "band", 0, 0, tiled=True)
    panel_all = got[:, :orb_dev].reshape(parts * orb_dev, share)
    image_all = got[:, orb_dev:].reshape(parts * orb_dev, share)
    s_part = contract(panel_all, panel_all)
    h_part = contract(image_all, panel_all)
    tiles = jnp.stack([s_part, h_part]).reshape(2, parts, orb_dev, parts * orb_dev)
    got = lax.all_to_all(tiles.transpose(1, 0, 2, 3), "band", 0, 0, tiled=True)
    rows = jnp.sum(got, axis=0)
    count = lax.axis_size("domain")
    sent = jnp.broadcast_to(rows[None], (count,) + rows.shape)
    got = lax.all_to_all(sent, "domain", 0, 0, tiled=True)
    return jnp.sum(got, axis=0)


def halo_of(fields, depths, planes):
    count = lax.axis_size("domain")
    reach = max(depths)
    blocks = -(-reach // planes)
    lefts = [[] for _ in fields]
    rights = [[] for _ in fields]
    for shift in range(1, blocks + 1):
        wanted = [i for i, depth in enumerate(depths) if depth > (shift - 1) * planes]
        packed = jnp.concatenate([fields[i] for i in wanted], axis=0)
        from_left = lax.ppermute(packed, "domain", [(i, (i + shift) % count) for i in range(count)])
        from_right = lax.ppermute(packed, "domain", [(i, (i - shift) % count) for i in range(count)])
        row = 0
        for i in wanted:
            rows = fields[i].shape[0]
            lefts[i].insert(0, from_left[row : row + rows])
            rights[i].append(from_right[row : row + rows])
            row += rows
    out = []
    for i, depth in enumerate(depths):
        wide = jnp.concatenate(lefts[i] + [fields[i]] + rights[i], axis=1)
        cut = len(lefts[i]) * planes - depth
        out.append(lax.slice_in_dim(wide, cut, wide.shape[1] - cut, axis=1))
    return out


def crop(field, depth):
    return lax.slice_in_dim(field, depth, field.shape[1] - depth, axis=1)


def laplace_inner(grid_field):
    planes = grid_field.shape[1] - 2 * stencil_reach
    size_y = grid_field.shape[2]
    size_z = grid_field.shape[3]
    inner = crop(grid_field, stencil_reach)
    padded_yz = jnp.pad(
        inner, ((0, 0), (0, 0), (stencil_reach, stencil_reach), (stencil_reach, stencil_reach))
    )
    summed = 3.0 * stencil_coeffs[0] * inner
    for offset in range(1, stencil_reach + 1):
        along_x = (
            grid_field[:, stencil_reach + offset : stencil_reach + offset + planes]
            + grid_field[:, stencil_reach - offset : stencil_reach - offset + planes]
        )
        along_y = (
            padded_yz[
                :,
                :,
                stencil_reach + offset : stencil_reach + offset + size_y,
                stencil_reach : stencil_reach + size_z,
            ]
            + padded_yz[
                :,
                :,
                stencil_reach - offset : stencil_reach - offset + size_y,
                stencil_reach : stencil_reach + size_z,
            ]
        )
        along_z = (
            padded_yz[
                :,
                :,
                stencil_reach : stencil_reach + size_y,
                stencil_reach + offset : stencil_reach + offset + size_z,
            ]
            + padded_yz[
                :,
                :,
                stencil_reach : stencil_reach + size_y,
                stencil_reach - offset : stencil_reach - offset + size_z,
            ]
        )
        summed = summed + stencil_coeffs[offset] * (along_x + along_y + along_z)
    return summed


def hamiltonian_inner(grid_field, wide_pot):
    inner = crop(grid_field, stencil_reach)
    cut = (wide_pot.shape[0] - inner.shape[1]) // 2
    pot = lax.slice_in_dim(wide_pot, cut, wide_pot.shape[0] - cut, axis=0)
    return -0.5 * laplace_inner(grid_field) + pot[None] * inner


def body(orbitals, potential):
    local_pot = gather_potential(potential)
    planes = orbitals.shape[1]
    half_width = (upper_bound - lower_bound) / 2.0
    centre = (upper_bound + lower_bound) / 2.0
    sigma_first = half_width / (lowest_bound - centre)
    per_phase = 2
    applications = DEGREE + 1
    pot_depth = stencil_reach * (per_phase - 1)
    current, wide_pot = halo_of([orbitals, local_pot[None]], [stencil_reach * per_phase, pot_depth], planes)
    wide_pot = wide_pot[0]
    previous = None
    sigma_now = sigma_first
    step = 0
    h_image = None
    while step < applications:
        if step > 0:
            todo = min(per_phase, applications - step)
            if previous is not None and step < DEGREE:
                current, previous = halo_of(
                    [current, previous], [stencil_reach * todo, stencil_reach * (todo - 1)], planes
                )
            else:
                (current,) = halo_of([current], [stencil_reach * todo], planes)
        else:
            todo = per_phase
        for _ in range(todo):
            if step == 0:
                previous = current
                current = (hamiltonian_inner(current, wide_pot) - centre * crop(current, stencil_reach)) * (
                    sigma_first / half_width
                )
            elif step < DEGREE:
                sigma_next = 1.0 / (2.0 / sigma_first - sigma_now)
                inner = crop(current, stencil_reach)
                lag = (previous.shape[1] - inner.shape[1]) // 2
                update = (hamiltonian_inner(current, wide_pot) - centre * inner) * (
                    2.0 * sigma_next / half_width
                ) - sigma_now * sigma_next * crop(previous, lag)
                previous = current
                current = update
                sigma_now = sigma_next
            else:
                h_image = hamiltonian_inner(current, wide_pot)
            step += 1
        if step < applications:
            lag = (previous.shape[1] - planes) // 2
            previous = crop(previous, lag)
    depth = (current.shape[1] - planes) // 2
    current = crop(current, depth)
    orb_dev = current.shape[0]
    cell_count = current.shape[1] * current.shape[2] * current.shape[3] * lax.axis_size("domain")
    totals = gram_rows(current.reshape(orb_dev, -1), h_image.reshape(orb_dev, -1))
    intersection = totals[0] / cell_count
    hamiltonian = totals[1] / cell_count
    return (current, intersection, hamiltonian)


def solution(mesh):
    placed = (P("band", "domain", None, None), P("domain", None, "band"))
    return jax.shard_map(
        body,
        mesh=mesh,
        in_specs=placed,
        out_specs=(P("band", "domain", None, None), P("band", None), P("band", None)),
        check_vma=False,
    )
```
